512 devices in a mesh: grp: 8 (over y_lo, core), own: 64 (over x, y_hi, z).
Axes of the slice: x: 4, y: 8 (y_hi: 2, y_lo: 4; y = y_hi * 4 + y_lo), z: 8, core: 2. Of those that a mesh axis runs over, the one named last changes fastest.
Arguments:
- activations: bfloat16 [65536, 1024], P(('grp', 'own'))
- out_grads: bfloat16 [65536, 1024], P(('grp', 'own')), may hold values from -0.01953125 to 0.01953125
- master: float32 [1024, 1024], P('own'), may hold values from -6 to 6
- moment: float32 [1024, 1024], P('own'), may hold values from 0.05 to 5
- left_root: bfloat16 [1024, 1024], P('own'), may hold values from -0.25 to 2.25, as said below
- right_root: bfloat16 [1024, 1024], P('own'), may hold values from -0.25 to 2.25, as said below
- stats_in: float32 [256, 16, 1024], P('own'), may hold values from -6 to 6
- tile_slot: int32 [128], replicated, may hold values from 0 to 255, as said below
Outputs:
- master_out: float32 [1024, 1024], P('own')
- moment_out: float32 [1024, 1024], P('own')
- stats_out: float32 [256, 16, 1024], P('own')
- weights: bfloat16 [1024, 1024], replicated
The draws below stay inside these ranges and needn't reach their ends.
Inputs may be any that keep to these rules, and one draw needn't show every extreme that they name: `tile_slot`: distinct slot numbers; slot s belongs to owner s // 4; some owner holds 4 tiles. `left_root`: symmetric. `right_root`: symmetric.
All inputs are finite; a program needn't handle non-finite values.
Results may differ from the reference program's by a relative error of at most 0.005.
Values may be sent and summed in bfloat16 or wider, within the bound.
No kernel may reach another device: no remote copies, remote signals or barrier semaphores. Data moves between devices by JAX's collectives and lax.ppermute only.
A program may use at most 64 MiB of HBM per device.

```python
import math
import jax
import jax.numpy as jnp
from jax import lax

BLOCK = 1024
TILE_ROWS = 16
TILES = 128
CAP = 4
SLOTS = 256
TOKENS_ALL = 65536


def draw_activations(key, part):
    sample_key = jax.random.fold_in(key, 5)
    position = jnp.arange(BLOCK, dtype=jnp.float32) / (BLOCK - 1)
    samples = jax.random.normal(sample_key, (TOKENS_ALL, BLOCK), jnp.float32)
    col_scale = 10.0 ** position
    return (samples * col_scale[None, :]).astype(jnp.bfloat16)


def draw_root_matrix(key):
    key_spread, key_diagonal = jax.random.split(key)
    spread = jax.random.normal(key_spread, (BLOCK, BLOCK), jnp.float32) * (0.5 / BLOCK ** 0.5)
    symmetric = (spread + spread.T) * 0.5
    diagonal = jax.random.uniform(key_diagonal, (BLOCK,), jnp.float32, 0.5, 1.5)
    row_ids = jnp.arange(BLOCK)
    on_diagonal = row_ids[:, None] == row_ids[None, :]
    return (symmetric + jnp.where(on_diagonal, diagonal[None, :], 0.0)).astype(jnp.bfloat16)


def draw_left_root(key, part):
    return draw_root_matrix(jax.random.fold_in(key, 11))


def draw_right_root(key, part):
    return draw_root_matrix(jax.random.fold_in(key, 23))


def draw_tile_slot(key, part):
    key_owner, key_ranking, key_shuffle = jax.random.split(jax.random.fold_in(key, 7), 3)
    full_owner = jax.random.randint(key_owner, (), 0, SLOTS // CAP).astype(jnp.int32)
    slot_ids = jnp.arange(SLOTS, dtype=jnp.int32)
    owners_of = slot_ids // CAP
    ranking = jax.random.permutation(key_ranking, SLOTS).astype(jnp.int32)
    end_slots = ((slot_ids == 0) | (slot_ids == SLOTS - 1)) & (owners_of != full_owner)
    priority = ranking + SLOTS * (owners_of == full_owner).astype(jnp.int32) - 2 * SLOTS * end_slots.astype(jnp.int32)
    ranked = jnp.argsort(priority).astype(jnp.int32)
    chosen = jnp.concatenate([full_owner * CAP + jnp.arange(CAP, dtype=jnp.int32), ranked[:TILES - CAP]])
    shuffle = jax.random.permutation(key_shuffle, TILES)
    return chosen[shuffle].astype(jnp.int32)


def steps_of(key, extent, cuts, low, top_value):
    def one(dim, blocks):
        heights = jax.random.uniform(jax.random.fold_in(jax.random.fold_in(key, 6), dim), (blocks,), jnp.float32, low / len(cuts), top_value / len(cuts))
        return jnp.repeat(jnp.exp(heights), extent[dim] // blocks).reshape((-1,) + (1,) * (len(extent) - dim - 1))

    level = one(*cuts[0])
    for cut in cuts[1:]:
        level = level * one(*cut)
    return level


def scatter_about(stream_key, shape, width, bound, shards=(), kind=jnp.bfloat16):
    result = jax.random.normal(stream_key, shape, jnp.float32) * width
    if len(shards) > 0:
        result = steps_of(stream_key, shape, shards, -0.22, 0.18) * result
    return jnp.clip(result, min=-bound, max=bound).astype(kind)


def setup_inputs(seed: int = 0) -> dict:
    keys = jax.random.split(jax.random.key(seed), 9)
    activations = draw_activations(jax.random.fold_in(keys[8], 71), 0)
    out_grads = scatter_about(keys[1], (TOKENS_ALL, BLOCK), (TOKENS_ALL ** -0.5 / 3), 0.01953125, ((0, 512),))
    master = scatter_about(keys[2], (BLOCK, BLOCK), 0.5, 6.0, ((0, 64),), jnp.float32)
    moment = jnp.clip(jnp.exp(math.log(5.0) - 4.6051702 * jax.random.uniform(keys[3], (BLOCK, BLOCK), jnp.float32) ** steps_of(keys[3], (BLOCK, BLOCK), ((0, 64),), -0.2, 0.2)), 0.05, 5.0)
    left_root = draw_left_root(jax.random.fold_in(keys[8], 71), 0)
    right_root = draw_right_root(jax.random.fold_in(keys[8], 71), 0)
    stats_in = scatter_about(keys[6], (SLOTS, TILE_ROWS, BLOCK), 1.0, 6.0, ((0, 64),), jnp.float32)
    tile_slot = draw_tile_slot(jax.random.fold_in(keys[8], 71), 0)
    return dict(activations=activations, out_grads=out_grads, master=master, moment=moment, left_root=left_root, right_root=right_root, stats_in=stats_in, tile_slot=tile_slot)


stat_decay = 0.9
moment_decay = 0.95
learn_rate = 0.3
adam_eps = 1e-08
norm_eps = 1e-06

def reference(activations, out_grads, master, moment, left_root, right_root, stats_in, tile_slot):
    gradient = lax.dot_general(activations, out_grads, (((0,), (0,)), ((), ())), preferred_element_type=jnp.float32)
    moment_out = moment_decay * moment + (1.0 - moment_decay) * gradient * gradient
    adam_dir = gradient / (jnp.sqrt(moment_out) + adam_eps)
    left_stat = lax.dot_general(gradient, gradient, (((1,), (1,)), ((), ())), precision=lax.Precision.HIGHEST, preferred_element_type=jnp.float32)
    right_stat = lax.dot_general(gradient, gradient, (((0,), (0,)), ((), ())), precision=lax.Precision.HIGHEST, preferred_element_type=jnp.float32)
    stacked = jnp.concatenate([left_stat, right_stat], axis=0).reshape(TILES, TILE_ROWS, BLOCK)
    fresh_tiles = stat_decay * stats_in[tile_slot] + (1.0 - stat_decay) / BLOCK * stacked
    stats_out = jnp.zeros_like(stats_in).at[tile_slot].set(fresh_tiles)
    grad_low = gradient.astype(jnp.bfloat16)
    left_mid = jnp.dot(left_root, grad_low, preferred_element_type=jnp.float32).astype(jnp.bfloat16)
    precond = jnp.dot(left_mid, right_root, preferred_element_type=jnp.float32)
    graft_scale = jnp.sqrt(jnp.sum(adam_dir * adam_dir)) / (jnp.sqrt(jnp.sum(precond * precond)) + norm_eps)
    master_out = master - learn_rate * graft_scale * precond
    return (master_out, moment_out, stats_out, master_out.astype(jnp.bfloat16))
```

```python
import jax
import jax.numpy as jnp
from jax import lax
from jax.sharding import Mesh
from jax.sharding import PartitionSpec as P

stat_decay = 0.9
moment_decay = 0.95
learn_rate = 0.3
adam_eps = 1e-08
norm_eps = 1e-06

GRP = ("yl", "c")
OWN = ("x", "yh", "z")
SUB_SIZES = (4, 2, 4, 2, 8)


def split3(value):
    hi = lax.reduce_precision(value, exponent_bits=8, mantissa_bits=7)
    rest = value - hi
    mid = lax.reduce_precision(rest, exponent_bits=8, mantissa_bits=7)
    lo = lax.reduce_precision(rest - mid, exponent_bits=8, mantissa_bits=7)
    return jnp.stack([hi, mid, lo])


def gather_own_rows(block):
    rows = block.shape[0]
    out = block
    for axis in ("yh", "x", "z"):
        out = lax.all_gather(out, axis, axis=0, tiled=True)
    out = out.reshape(SUB_SIZES[4], SUB_SIZES[2], SUB_SIZES[3], rows, block.shape[1])
    out = jnp.transpose(out, (1, 2, 0, 3, 4))
    return out.reshape(-1, block.shape[1])


def local(activations, out_grads, master, moment, left_root, right_root, stats_in, tile_slot):
    owner_rows = master.shape[0]
    block_size = master.shape[1]
    owners = block_size // owner_rows
    capacity = stats_in.shape[0]
    tile_rows = stats_in.shape[1]
    tile_count = tile_slot.shape[0]
    owner_index = lax.axis_index(OWN)
    grp_size = SUB_SIZES[0] * SUB_SIZES[1]

    left_full = gather_own_rows(left_root)
    right_full = gather_own_rows(right_root)
    master_full = gather_own_rows(master)

    partial = lax.dot_general(
        activations, out_grads, (((0,), (0,)), ((), ())), preferred_element_type=jnp.float32
    )
    pieces = lax.all_to_all(
        partial.reshape(owners, owner_rows, block_size), OWN, 0, 0, tiled=True
    )
    own_sum = jnp.sum(pieces, axis=0)
    copies = jnp.broadcast_to(own_sum[None], (grp_size, owner_rows, block_size))
    grad_rows = jnp.sum(lax.all_to_all(copies, GRP, 0, 0, tiled=True), axis=0)

    moment_out = moment_decay * moment + (1.0 - moment_decay) * grad_rows * grad_rows
    adam_dir = grad_rows / (jnp.sqrt(moment_out) + adam_eps)
    adam_part = split3(jnp.sum(adam_dir * adam_dir))

    extra = jnp.zeros((1, block_size), jnp.float32).at[0, :3].set(adam_part)
    payload = jnp.concatenate([grad_rows, extra], axis=0).astype(jnp.bfloat16)
    sent = jnp.broadcast_to(payload[None], (owners,) + payload.shape)
    got = lax.all_to_all(sent, OWN, 0, 0, tiled=True)
    grad_low = got[:, :owner_rows, :].reshape(block_size, block_size)
    adam_sum = jnp.sum(got[:, owner_rows, :3].astype(jnp.float32))

    left_mid = jnp.dot(left_full, grad_low, preferred_element_type=jnp.float32).astype(jnp.bfloat16)
    precond = jnp.dot(left_mid, right_full, preferred_element_type=jnp.float32)
    graft_scale = jnp.sqrt(adam_sum) / (jnp.sqrt(jnp.sum(precond * precond)) + norm_eps)
    master_out_full = master_full - learn_rate * graft_scale * precond
    weights = master_out_full.astype(jnp.bfloat16)
    master_out = lax.dynamic_slice_in_dim(master_out_full, owner_index * owner_rows, owner_rows, 0)

    my_slots = owner_index * capacity + jnp.arange(capacity, dtype=jnp.int32)
    matches = (tile_slot[:, None] == my_slots[None, :]).astype(jnp.int32)
    tile_ids = jnp.sum(matches * jnp.arange(tile_count, dtype=jnp.int32)[:, None], axis=0)
    filled = jnp.sum(matches, axis=0)
    per_half = block_size // tile_rows
    which_half = tile_ids // per_half
    offsets = (tile_ids - which_half * per_half) * tile_rows
    grad_low_t = grad_low.T
    row_blocks = jnp.concatenate(
        [lax.dynamic_slice_in_dim(grad_low, offsets[s], tile_rows, 0) for s in range(capacity)], axis=0
    )
    col_blocks = jnp.concatenate(
        [lax.dynamic_slice_in_dim(grad_low_t, offsets[s], tile_rows, 0) for s in range(capacity)], axis=0
    )
    left_tiles = lax.dot_general(
        row_blocks, grad_low, (((1,), (1,)), ((), ())), preferred_element_type=jnp.float32
    ).reshape(capacity, tile_rows, block_size)
    right_tiles = jnp.dot(col_blocks, grad_low, preferred_element_type=jnp.float32).reshape(
        capacity, tile_rows, block_size
    )
    product = jnp.where((which_half == 0)[:, None, None], left_tiles, right_tiles)
    fresh = stat_decay * stats_in + (1.0 - stat_decay) / block_size * product
    stats_out = jnp.where((filled > 0)[:, None, None], fresh, 0.0)
    return (master_out, moment_out, stats_out, weights)


def solution(mesh):
    sub_mesh = Mesh(mesh.devices.reshape(SUB_SIZES), GRP + OWN)
    rows_all = P(GRP + OWN, None)
    rows_own = P(OWN, None)
    in_specs = (rows_all, rows_all, rows_own, rows_own, rows_own, rows_own, P(OWN, None, None), P())
    out_specs = (rows_own, rows_own, P(OWN, None, None), P())
    return jax.shard_map(local, mesh=sub_mesh, in_specs=in_specs, out_specs=out_specs, check_vma=False)
```

```python
import jax
import jax.numpy as jnp
from jax import lax
from jax.sharding import Mesh
from jax.sharding import PartitionSpec as P

stat_decay = 0.9
moment_decay = 0.95
learn_rate = 0.3
adam_eps = 1e-08
norm_eps = 1e-06

GRP = ("yl", "c")
OWN = ("x", "yh", "z")
SUB_SIZES = (4, 2, 4, 2, 8)


def split3(value):
    hi = lax.reduce_precision(value, exponent_bits=8, mantissa_bits=7)
    rest = value - hi
    mid = lax.reduce_precision(rest, exponent_bits=8, mantissa_bits=7)
    lo = lax.reduce_precision(rest - mid, exponent_bits=8, mantissa_bits=7)
    return jnp.stack([hi, mid, lo])


def gather_own_rows(block):
    rows = block.shape[0]
    out = block
    for axis in ("yh", "x", "z"):
        out = lax.all_gather(out, axis, axis=0, tiled=True)
    out = out.reshape(SUB_SIZES[4], SUB_SIZES[2], SUB_SIZES[3], rows, block.shape[1])
    out = jnp.transpose(out, (1, 2, 0, 3, 4))
    return out.reshape(-1, block.shape[1])


def local(activations, out_grads, master, moment, left_root, right_root, stats_in, tile_slot):
    owner_rows = master.shape[0]
    block_size = master.shape[1]
    owners = block_size // owner_rows
    capacity = stats_in.shape[0]
    tile_rows = stats_in.shape[1]
    tile_count = tile_slot.shape[0]
    owner_index = lax.axis_index(OWN)
    grp_size = SUB_SIZES[0] * SUB_SIZES[1]

    right_full = gather_own_rows(right_root)

    partial = lax.dot_general(
        activations, out_grads, (((0,), (0,)), ((), ())), preferred_element_type=jnp.float32
    )
    pieces = lax.all_to_all(
        partial.reshape(owners, owner_rows, block_size), OWN, 0, 0, tiled=True
    )
    own_sum = jnp.sum(pieces, axis=0)
    copies = jnp.broadcast_to(own_sum[None], (grp_size, owner_rows, block_size))
    grad_rows = jnp.sum(lax.all_to_all(copies, GRP, 0, 0, tiled=True), axis=0)

    moment_out = moment_decay * moment + (1.0 - moment_decay) * grad_rows * grad_rows
    adam_dir = grad_rows / (jnp.sqrt(moment_out) + adam_eps)
    adam_part = split3(jnp.sum(adam_dir * adam_dir))

    extra = jnp.zeros((1, block_size), jnp.float32).at[0, :3].set(adam_part)
    payload = jnp.concatenate([grad_rows, extra], axis=0).astype(jnp.bfloat16)
    sent = jnp.broadcast_to(payload[None], (owners,) + payload.shape)
    got = lax.all_to_all(sent, OWN, 0, 0, tiled=True)
    grad_low = got[:, :owner_rows, :].reshape(block_size, block_size)
    adam_sum = jnp.sum(got[:, owner_rows, :3].astype(jnp.float32))

    left_mid = jnp.dot(left_root, grad_low, preferred_element_type=jnp.float32).astype(jnp.bfloat16)
    precond = jnp.dot(left_mid, right_full, preferred_element_type=jnp.float32)
    precond_part = jnp.broadcast_to(jnp.sum(precond * precond), (owners, 1, 128))
    precond_sum = jnp.sum(lax.all_to_all(precond_part, OWN, 0, 0, tiled=True)[:, 0, 0])
    graft_scale = jnp.sqrt(adam_sum) / (jnp.sqrt(precond_sum) + norm_eps)
    master_out = master - learn_rate * graft_scale * precond
    weight_rows = jnp.broadcast_to(master_out.astype(jnp.bfloat16)[None], (owners, owner_rows, block_size))
    weights = lax.all_to_all(weight_rows, OWN, 0, 0, tiled=True).reshape(block_size, block_size)

    my_slots = owner_index * capacity + jnp.arange(capacity, dtype=jnp.int32)
    matches = (tile_slot[:, None] == my_slots[None, :]).astype(jnp.int32)
    tile_ids = jnp.sum(matches * jnp.arange(tile_count, dtype=jnp.int32)[:, None], axis=0)
    filled = jnp.sum(matches, axis=0)
    per_half = block_size // tile_rows
    which_half = tile_ids // per_half
    offsets = (tile_ids - which_half * per_half) * tile_rows
    grad_low_t = grad_low.T
    row_blocks = jnp.concatenate(
        [lax.dynamic_slice_in_dim(grad_low, offsets[s], tile_rows, 0) for s in range(capacity)], axis=0
    )
    col_blocks = jnp.concatenate(
        [lax.dynamic_slice_in_dim(grad_low_t, offsets[s], tile_rows, 0) for s in range(capacity)], axis=0
    )
    left_tiles = lax.dot_general(
        row_blocks, grad_low, (((1,), (1,)), ((), ())), preferred_element_type=jnp.float32
    ).reshape(capacity, tile_rows, block_size)
    right_tiles = jnp.dot(col_blocks, grad_low, preferred_element_type=jnp.float32).reshape(
        capacity, tile_rows, block_size
    )
    product = jnp.where((which_half == 0)[:, None, None], left_tiles, right_tiles)
    fresh = stat_decay * stats_in + (1.0 - stat_decay) / block_size * product
    stats_out = jnp.where((filled > 0)[:, None, None], fresh, 0.0)
    return (master_out, moment_out, stats_out, weights)


def solution(mesh):
    sub_mesh = Mesh(mesh.devices.reshape(SUB_SIZES), GRP + OWN)
    rows_all = P(GRP + OWN, None)
    rows_own = P(OWN, None)
    in_specs = (rows_all, rows_all, rows_own, rows_own, rows_own, rows_own, P(OWN, None, None), P())
    out_specs = (rows_own, rows_own, P(OWN, None, None), P())
    return jax.shard_map(local, mesh=sub_mesh, in_specs=in_specs, out_specs=out_specs, check_vma=False)
```

```python
import jax
import jax.numpy as jnp
from jax import lax
from jax.sharding import Mesh
from jax.sharding import PartitionSpec as P

stat_decay = 0.9
moment_decay = 0.95
learn_rate = 0.3
adam_eps = 1e-08
norm_eps = 1e-06

GRP = ("yl", "c")
OWN = ("x", "yh", "z")
SUB_SIZES = (4, 2, 4, 2, 8)


def split3(value):
    hi = lax.reduce_precision(value, exponent_bits=8, mantissa_bits=7)
    rest = value - hi
    mid = lax.reduce_precision(rest, exponent_bits=8, mantissa_bits=7)
    lo = lax.reduce_precision(rest - mid, exponent_bits=8, mantissa_bits=7)
    return jnp.stack([hi, mid, lo])


def gather_own_rows(block):
    rows = block.shape[0]
    out = block
    for axis in ("yh", "x", "z"):
        out = lax.all_gather(out, axis, axis=0, tiled=True)
    out = out.reshape(SUB_SIZES[4], SUB_SIZES[2], SUB_SIZES[3], rows, block.shape[1])
    out = jnp.transpose(out, (1, 2, 0, 3, 4))
    return out.reshape(-1, block.shape[1])


def local(activations, out_grads, master, moment, left_root, right_root, stats_in, tile_slot):
    owner_rows = master.shape[0]
    block_size = master.shape[1]
    owners = block_size // owner_rows
    capacity = stats_in.shape[0]
    tile_rows = stats_in.shape[1]
    tile_count = tile_slot.shape[0]
    owner_index = lax.axis_index(OWN)
    grp_size = SUB_SIZES[0] * SUB_SIZES[1]


    partial = lax.dot_general(
        activations, out_grads, (((0,), (0,)), ((), ())), preferred_element_type=jnp.float32
    )
    pieces = lax.all_to_all(
        partial.reshape(owners, owner_rows, block_size), OWN, 0, 0, tiled=True
    )
    own_sum = jnp.sum(pieces, axis=0)
    copies = jnp.broadcast_to(own_sum[None], (grp_size, owner_rows, block_size))
    grad_rows = jnp.sum(lax.all_to_all(copies, GRP, 0, 0, tiled=True), axis=0)

    moment_out = moment_decay * moment + (1.0 - moment_decay) * grad_rows * grad_rows
    adam_dir = grad_rows / (jnp.sqrt(moment_out) + adam_eps)
    adam_part = split3(jnp.sum(adam_dir * adam_dir))

    extra = jnp.zeros((1, block_size), jnp.float32).at[0, :3].set(adam_part)
    payload = jnp.concatenate(
        [grad_rows.astype(jnp.bfloat16), extra.astype(jnp.bfloat16), right_root], axis=0
    )
    sent = jnp.broadcast_to(payload[None], (owners,) + payload.shape)
    got = lax.all_to_all(sent, OWN, 0, 0, tiled=True)
    grad_low = got[:, :owner_rows, :].reshape(block_size, block_size)
    adam_sum = jnp.sum(got[:, owner_rows, :3].astype(jnp.float32))
    right_full = got[:, owner_rows + 1 :, :].reshape(block_size, block_size)

    left_mid = jnp.dot(left_root, grad_low, preferred_element_type=jnp.float32).astype(jnp.bfloat16)
    precond = jnp.dot(left_mid, right_full, preferred_element_type=jnp.float32)
    precond_part = jnp.broadcast_to(jnp.sum(precond * precond), (owners, 1, 128))
    precond_sum = jnp.sum(lax.all_to_all(precond_part, OWN, 0, 0, tiled=True)[:, 0, 0])
    graft_scale = jnp.sqrt(adam_sum) / (jnp.sqrt(precond_sum) + norm_eps)
    master_out = master - learn_rate * graft_scale * precond
    weight_rows = jnp.broadcast_to(master_out.astype(jnp.bfloat16)[None], (owners, owner_rows, block_size))
    weights = lax.all_to_all(weight_rows, OWN, 0, 0, tiled=True).reshape(block_size, block_size)

    my_slots = owner_index * capacity + jnp.arange(capacity, dtype=jnp.int32)
    matches = (tile_slot[:, None] == my_slots[None, :]).astype(jnp.int32)
    tile_ids = jnp.sum(matches * jnp.arange(tile_count, dtype=jnp.int32)[:, None], axis=0)
    filled = jnp.sum(matches, axis=0)
    per_half = block_size // tile_rows
    which_half = tile_ids // per_half
    offsets = (tile_ids - which_half * per_half) * tile_rows
    grad_low_t = grad_low.T
    row_blocks = jnp.concatenate(
        [lax.dynamic_slice_in_dim(grad_low, offsets[s], tile_rows, 0) for s in range(capacity)], axis=0
    )
    col_blocks = jnp.concatenate(
        [lax.dynamic_slice_in_dim(grad_low_t, offsets[s], tile_rows, 0) for s in range(capacity)], axis=0
    )
    left_tiles = lax.dot_general(
        row_blocks, grad_low, (((1,), (1,)), ((), ())), preferred_element_type=jnp.float32
    ).reshape(capacity, tile_rows, block_size)
    right_tiles = jnp.dot(col_blocks, grad_low, preferred_element_type=jnp.float32).reshape(
        capacity, tile_rows, block_size
    )
    product = jnp.where((which_half == 0)[:, None, None], left_tiles, right_tiles)
    fresh = stat_decay * stats_in + (1.0 - stat_decay) / block_size * product
    stats_out = jnp.where((filled > 0)[:, None, None], fresh, 0.0)
    return (master_out, moment_out, stats_out, weights)


def solution(mesh):
    sub_mesh = Mesh(mesh.devices.reshape(SUB_SIZES), GRP + OWN)
    rows_all = P(GRP + OWN, None)
    rows_own = P(OWN, None)
    in_specs = (rows_all, rows_all, rows_own, rows_own, rows_own, rows_own, P(OWN, None, None), P())
    out_specs = (rows_own, rows_own, P(OWN, None, None), P())
    return jax.shard_map(local, mesh=sub_mesh, in_specs=in_specs, out_specs=out_specs, check_vma=False)
```

```python
import jax
import jax.numpy as jnp
from jax import lax
from jax.sharding import Mesh
from jax.sharding import PartitionSpec as P

stat_decay = 0.9
moment_decay = 0.95
learn_rate = 0.3
adam_eps = 1e-08
norm_eps = 1e-06

GRP = ("yl", "c")
OWN = ("x", "yh", "z")
SUB_SIZES = (4, 2, 4, 2, 8)


def split3(value):
    hi = lax.reduce_precision(value, exponent_bits=8, mantissa_bits=7)
    rest = value - hi
    mid = lax.reduce_precision(rest, exponent_bits=8, mantissa_bits=7)
    lo = lax.reduce_precision(rest - mid, exponent_bits=8, mantissa_bits=7)
    return jnp.stack([hi, mid, lo])


def gather_own_rows(block):
    rows = block.shape[0]
    out = block
    for axis in ("yh", "x", "z"):
        out = lax.all_gather(out, axis, axis=0, tiled=True)
    out = out.reshape(SUB_SIZES[4], SUB_SIZES[2], SUB_SIZES[3], rows, block.shape[1])
    out = jnp.transpose(out, (1, 2, 0, 3, 4))
    return out.reshape(-1, block.shape[1])


def local(activations, out_grads, master, moment, left_root, right_root, stats_in, tile_slot):
    owner_rows = master.shape[0]
    block_size = master.shape[1]
    owners = block_size // owner_rows
    capacity = stats_in.shape[0]
    tile_rows = stats_in.shape[1]
    tile_count = tile_slot.shape[0]
    owner_index = lax.axis_index(OWN)
    grp_size = SUB_SIZES[0] * SUB_SIZES[1]


    with jax.named_scope("rgather"):
        right_full = lax.all_gather(right_root, OWN, axis=0, tiled=True)
    partial = lax.dot_general(
        activations, out_grads, (((0,), (0,)), ((), ())), preferred_element_type=jnp.float32
    )
    with jax.named_scope("reduce_a"):
        pieces = lax.all_to_all(
            partial.reshape(owners, owner_rows, block_size), OWN, 0, 0, tiled=True
        )
    own_sum = jnp.sum(pieces, axis=0)
    copies = jnp.broadcast_to(own_sum[None], (grp_size, owner_rows, block_size))
    grad_rows = jnp.sum(lax.all_to_all(copies, GRP, 0, 0, tiled=True), axis=0)

    moment_out = moment_decay * moment + (1.0 - moment_decay) * grad_rows * grad_rows
    adam_dir = grad_rows / (jnp.sqrt(moment_out) + adam_eps)
    adam_part = split3(jnp.sum(adam_dir * adam_dir))

    extra = jnp.zeros((1, block_size), jnp.float32).at[0, :3].set(adam_part)
    payload = jnp.concatenate([grad_rows, extra], axis=0).astype(jnp.bfloat16)
    sent = jnp.broadcast_to(payload[None], (owners,) + payload.shape)
    got = lax.all_to_all(sent, OWN, 0, 0, tiled=True)
    grad_low = got[:, :owner_rows, :].reshape(block_size, block_size)
    adam_sum = jnp.sum(got[:, owner_rows, :3].astype(jnp.float32))

    left_mid = jnp.dot(left_root, grad_low, preferred_element_type=jnp.float32).astype(jnp.bfloat16)
    precond = jnp.dot(left_mid, right_full, preferred_element_type=jnp.float32)
    precond_part = jnp.broadcast_to(jnp.sum(precond * precond), (owners, 1, 128))
    precond_sum = jnp.sum(lax.all_to_all(precond_part, OWN, 0, 0, tiled=True)[:, 0, 0])
    graft_scale = jnp.sqrt(adam_sum) / (jnp.sqrt(precond_sum) + norm_eps)
    master_out = master - learn_rate * graft_scale * precond
    weight_rows = jnp.broadcast_to(master_out.astype(jnp.bfloat16)[None], (owners, owner_rows, block_size))
    weights = lax.all_to_all(weight_rows, OWN, 0, 0, tiled=True).reshape(block_size, block_size)

    my_slots = owner_index * capacity + jnp.arange(capacity, dtype=jnp.int32)
    matches = (tile_slot[:, None] == my_slots[None, :]).astype(jnp.int32)
    tile_ids = jnp.sum(matches * jnp.arange(tile_count, dtype=jnp.int32)[:, None], axis=0)
    filled = jnp.sum(matches, axis=0)
    per_half = block_size // tile_rows
    which_half = tile_ids // per_half
    offsets = (tile_ids - which_half * per_half) * tile_rows
    grad_low_t = grad_low.T
    row_blocks = jnp.concatenate(
        [lax.dynamic_slice_in_dim(grad_low, offsets[s], tile_rows, 0) for s in range(capacity)], axis=0
    )
    col_blocks = jnp.concatenate(
        [lax.dynamic_slice_in_dim(grad_low_t, offsets[s], tile_rows, 0) for s in range(capacity)], axis=0
    )
    left_tiles = lax.dot_general(
        row_blocks, grad_low, (((1,), (1,)), ((), ())), preferred_element_type=jnp.float32
    ).reshape(capacity, tile_rows, block_size)
    right_tiles = jnp.dot(col_blocks, grad_low, preferred_element_type=jnp.float32).reshape(
        capacity, tile_rows, block_size
    )
    product = jnp.where((which_half == 0)[:, None, None], left_tiles, right_tiles)
    fresh = stat_decay * stats_in + (1.0 - stat_decay) / block_size * product
    stats_out = jnp.where((filled > 0)[:, None, None], fresh, 0.0)
    return (master_out, moment_out, stats_out, weights)


def solution(mesh):
    sub_mesh = Mesh(mesh.devices.reshape(SUB_SIZES), GRP + OWN)
    rows_all = P(GRP + OWN, None)
    rows_own = P(OWN, None)
    in_specs = (rows_all, rows_all, rows_own, rows_own, rows_own, rows_own, P(OWN, None, None), P())
    out_specs = (rows_own, rows_own, P(OWN, None, None), P())
    return jax.shard_map(local, mesh=sub_mesh, in_specs=in_specs, out_specs=out_specs, check_vma=False)
```

```python
import jax
import jax.numpy as jnp
from jax import lax
from jax.sharding import Mesh
from jax.sharding import PartitionSpec as P

stat_decay = 0.9
moment_decay = 0.95
learn_rate = 0.3
adam_eps = 1e-08
norm_eps = 1e-06

GRP = ("yl", "c")
OWN = ("x", "yh", "z")
SUB_SIZES = (4, 2, 4, 2, 8)


def split3(value):
    hi = lax.reduce_precision(value, exponent_bits=8, mantissa_bits=7)
    rest = value - hi
    mid = lax.reduce_precision(rest, exponent_bits=8, mantissa_bits=7)
    lo = lax.reduce_precision(rest - mid, exponent_bits=8, mantissa_bits=7)
    return jnp.stack([hi, mid, lo])


def gather_own_rows(block):
    rows = block.shape[0]
    out = block
    for axis in ("yh", "x", "z"):
        out = lax.all_gather(out, axis, axis=0, tiled=True)
    out = out.reshape(SUB_SIZES[4], SUB_SIZES[2], SUB_SIZES[3], rows, block.shape[1])
    out = jnp.transpose(out, (1, 2, 0, 3, 4))
    return out.reshape(-1, block.shape[1])


def local(activations, out_grads, master, moment, left_root, right_root, stats_in, tile_slot):
    owner_rows = master.shape[0]
    block_size = master.shape[1]
    owners = block_size // owner_rows
    capacity = stats_in.shape[0]
    tile_rows = stats_in.shape[1]
    tile_count = tile_slot.shape[0]
    owner_index = lax.axis_index(OWN)
    grp_size = SUB_SIZES[0] * SUB_SIZES[1]


    with jax.named_scope("rgather"):
        right_full = lax.all_gather(right_root, OWN, axis=0, tiled=True)
    partial = lax.dot_general(
        activations, out_grads, (((0,), (0,)), ((), ())), preferred_element_type=jnp.float32
    )
    cores = SUB_SIZES[1]
    part_rows = owner_rows // cores
    halves = jnp.transpose(partial.reshape(owners, cores, part_rows, block_size), (1, 0, 2, 3))
    chip_sum = jnp.sum(lax.all_to_all(halves, "c", 0, 0, tiled=True), axis=0)
    pieces = lax.all_to_all(chip_sum, OWN, 0, 0, tiled=True)
    own_sum = jnp.sum(pieces, axis=0)
    copies = jnp.broadcast_to(own_sum[None], (grp_size, part_rows, block_size))
    got_grp = lax.all_to_all(copies, GRP, 0, 0, tiled=True).reshape(
        SUB_SIZES[0], cores, part_rows, block_size
    )
    grad_rows = jnp.sum(got_grp, axis=0).reshape(owner_rows, block_size)

    moment_out = moment_decay * moment + (1.0 - moment_decay) * grad_rows * grad_rows
    adam_dir = grad_rows / (jnp.sqrt(moment_out) + adam_eps)
    adam_part = split3(jnp.sum(adam_dir * adam_dir))

    extra = jnp.zeros((1, block_size), jnp.float32).at[0, :3].set(adam_part)
    payload = jnp.concatenate([grad_rows, extra], axis=0).astype(jnp.bfloat16)
    sent = jnp.broadcast_to(payload[None], (owners,) + payload.shape)
    got = lax.all_to_all(sent, OWN, 0, 0, tiled=True)
    grad_low = got[:, :owner_rows, :].reshape(block_size, block_size)
    adam_sum = jnp.sum(got[:, owner_rows, :3].astype(jnp.float32))

    left_mid = jnp.dot(left_root, grad_low, preferred_element_type=jnp.float32).astype(jnp.bfloat16)
    precond = jnp.dot(left_mid, right_full, preferred_element_type=jnp.float32)
    precond_part = jnp.broadcast_to(jnp.sum(precond * precond), (owners, 1, 128))
    precond_sum = jnp.sum(lax.all_to_all(precond_part, OWN, 0, 0, tiled=True)[:, 0, 0])
    graft_scale = jnp.sqrt(adam_sum) / (jnp.sqrt(precond_sum) + norm_eps)
    master_out = master - learn_rate * graft_scale * precond
    weight_rows = jnp.broadcast_to(master_out.astype(jnp.bfloat16)[None], (owners, owner_rows, block_size))
    weights = lax.all_to_all(weight_rows, OWN, 0, 0, tiled=True).reshape(block_size, block_size)

    my_slots = owner_index * capacity + jnp.arange(capacity, dtype=jnp.int32)
    matches = (tile_slot[:, None] == my_slots[None, :]).astype(jnp.int32)
    tile_ids = jnp.sum(matches * jnp.arange(tile_count, dtype=jnp.int32)[:, None], axis=0)
    filled = jnp.sum(matches, axis=0)
    per_half = block_size // tile_rows
    which_half = tile_ids // per_half
    offsets = (tile_ids - which_half * per_half) * tile_rows
    grad_low_t = grad_low.T
    row_blocks = jnp.concatenate(
        [lax.dynamic_slice_in_dim(grad_low, offsets[s], tile_rows, 0) for s in range(capacity)], axis=0
    )
    col_blocks = jnp.concatenate(
        [lax.dynamic_slice_in_dim(grad_low_t, offsets[s], tile_rows, 0) for s in range(capacity)], axis=0
    )
    left_tiles = lax.dot_general(
        row_blocks, grad_low, (((1,), (1,)), ((), ())), preferred_element_type=jnp.float32
    ).reshape(capacity, tile_rows, block_size)
    right_tiles = jnp.dot(col_blocks, grad_low, preferred_element_type=jnp.float32).reshape(
        capacity, tile_rows, block_size
    )
    product = jnp.where((which_half == 0)[:, None, None], left_tiles, right_tiles)
    fresh = stat_decay * stats_in + (1.0 - stat_decay) / block_size * product
    stats_out = jnp.where((filled > 0)[:, None, None], fresh, 0.0)
    return (master_out, moment_out, stats_out, weights)


def solution(mesh):
    sub_mesh = Mesh(mesh.devices.reshape(SUB_SIZES), GRP + OWN)
    rows_all = P(GRP + OWN, None)
    rows_own = P(OWN, None)
    in_specs = (rows_all, rows_all, rows_own, rows_own, rows_own, rows_own, P(OWN, None, None), P())
    out_specs = (rows_own, rows_own, P(OWN, None, None), P())
    return jax.shard_map(local, mesh=sub_mesh, in_specs=in_specs, out_specs=out_specs, check_vma=False)
```

```python
import jax
import jax.numpy as jnp
from jax import lax
from jax.sharding import Mesh
from jax.sharding import PartitionSpec as P

stat_decay = 0.9
moment_decay = 0.95
learn_rate = 0.3
adam_eps = 1e-08
norm_eps = 1e-06

GRP = ("yl", "c")
OWN = ("x", "yh", "z")
SUB_SIZES = (4, 2, 4, 2, 8)


def split3(value):
    hi = lax.reduce_precision(value, exponent_bits=8, mantissa_bits=7)
    rest = value - hi
    mid = lax.reduce_precision(rest, exponent_bits=8, mantissa_bits=7)
    lo = lax.reduce_precision(rest - mid, exponent_bits=8, mantissa_bits=7)
    return jnp.stack([hi, mid, lo])


def gather_own_rows(block):
    rows = block.shape[0]
    out = block
    for axis in ("yh", "x", "z"):
        out = lax.all_gather(out, axis, axis=0, tiled=True)
    out = out.reshape(SUB_SIZES[4], SUB_SIZES[2], SUB_SIZES[3], rows, block.shape[1])
    out = jnp.transpose(out, (1, 2, 0, 3, 4))
    return out.reshape(-1, block.shape[1])


def join_cores(parts, cores):
    both = lax.all_to_all(jnp.broadcast_to(parts[None], (cores,) + parts.shape), "c", 0, 0, tiled=True)
    return jnp.transpose(both, (1, 0, 2, 3)).reshape(-1, parts.shape[-1])


def local(activations, out_grads, master, moment, left_root, right_root, stats_in, tile_slot):
    owner_rows = master.shape[0]
    block_size = master.shape[1]
    owners = block_size // owner_rows
    capacity = stats_in.shape[0]
    tile_rows = stats_in.shape[1]
    tile_count = tile_slot.shape[0]
    owner_index = lax.axis_index(OWN)
    grp_size = SUB_SIZES[0] * SUB_SIZES[1]


    with jax.named_scope("rgather"):
        right_full = lax.all_gather(right_root, OWN, axis=0, tiled=True)
    partial = lax.dot_general(
        activations, out_grads, (((0,), (0,)), ((), ())), preferred_element_type=jnp.float32
    )
    cores = SUB_SIZES[1]
    part_rows = owner_rows // cores
    halves = jnp.transpose(partial.reshape(owners, cores, part_rows, block_size), (1, 0, 2, 3))
    chip_sum = jnp.sum(lax.all_to_all(halves, "c", 0, 0, tiled=True), axis=0)
    pieces = lax.all_to_all(chip_sum, OWN, 0, 0, tiled=True)
    own_sum = jnp.sum(pieces, axis=0)
    copies = jnp.broadcast_to(own_sum[None], (grp_size, part_rows, block_size))
    got_grp = lax.all_to_all(copies, GRP, 0, 0, tiled=True).reshape(
        SUB_SIZES[0], cores, part_rows, block_size
    )
    grad_rows = jnp.sum(got_grp, axis=0).reshape(owner_rows, block_size)

    moment_out = moment_decay * moment + (1.0 - moment_decay) * grad_rows * grad_rows
    adam_dir = grad_rows / (jnp.sqrt(moment_out) + adam_eps)
    adam_part = split3(jnp.sum(adam_dir * adam_dir))

    extra = jnp.zeros((1, block_size), jnp.float32).at[0, :3].set(adam_part)
    core = lax.axis_index("c")
    my_part = lax.dynamic_slice_in_dim(grad_rows, core * part_rows, part_rows, 0)
    payload = jnp.concatenate([my_part, extra], axis=0).astype(jnp.bfloat16)
    sent = jnp.broadcast_to(payload[None], (owners,) + payload.shape)
    got = lax.all_to_all(sent, OWN, 0, 0, tiled=True)
    grad_low = join_cores(got[:, :part_rows, :], cores)
    adam_sum = jnp.sum(got[:, part_rows, :3].astype(jnp.float32))

    left_mid = jnp.dot(left_root, grad_low, preferred_element_type=jnp.float32).astype(jnp.bfloat16)
    precond = jnp.dot(left_mid, right_full, preferred_element_type=jnp.float32)
    precond_part = jnp.broadcast_to(jnp.sum(precond * precond), (owners, 1, 128))
    precond_sum = jnp.sum(lax.all_to_all(precond_part, OWN, 0, 0, tiled=True)[:, 0, 0])
    graft_scale = jnp.sqrt(adam_sum) / (jnp.sqrt(precond_sum) + norm_eps)
    master_out = master - learn_rate * graft_scale * precond
    weight_part = lax.dynamic_slice_in_dim(master_out.astype(jnp.bfloat16), core * part_rows, part_rows, 0)
    weight_rows = jnp.broadcast_to(weight_part[None], (owners, part_rows, block_size))
    weights = join_cores(lax.all_to_all(weight_rows, OWN, 0, 0, tiled=True), cores)

    my_slots = owner_index * capacity + jnp.arange(capacity, dtype=jnp.int32)
    matches = (tile_slot[:, None] == my_slots[None, :]).astype(jnp.int32)
    tile_ids = jnp.sum(matches * jnp.arange(tile_count, dtype=jnp.int32)[:, None], axis=0)
    filled = jnp.sum(matches, axis=0)
    per_half = block_size // tile_rows
    which_half = tile_ids // per_half
    offsets = (tile_ids - which_half * per_half) * tile_rows
    grad_low_t = grad_low.T
    row_blocks = jnp.concatenate(
        [lax.dynamic_slice_in_dim(grad_low, offsets[s], tile_rows, 0) for s in range(capacity)], axis=0
    )
    col_blocks = jnp.concatenate(
        [lax.dynamic_slice_in_dim(grad_low_t, offsets[s], tile_rows, 0) for s in range(capacity)], axis=0
    )
    left_tiles = lax.dot_general(
        row_blocks, grad_low, (((1,), (1,)), ((), ())), preferred_element_type=jnp.float32
    ).reshape(capacity, tile_rows, block_size)
    right_tiles = jnp.dot(col_blocks, grad_low, preferred_element_type=jnp.float32).reshape(
        capacity, tile_rows, block_size
    )
    product = jnp.where((which_half == 0)[:, None, None], left_tiles, right_tiles)
    fresh = stat_decay * stats_in + (1.0 - stat_decay) / block_size * product
    stats_out = jnp.where((filled > 0)[:, None, None], fresh, 0.0)
    return (master_out, moment_out, stats_out, weights)


def solution(mesh):
    sub_mesh = Mesh(mesh.devices.reshape(SUB_SIZES), GRP + OWN)
    rows_all = P(GRP + OWN, None)
    rows_own = P(OWN, None)
    in_specs = (rows_all, rows_all, rows_own, rows_own, rows_own, rows_own, P(OWN, None, None), P())
    out_specs = (rows_own, rows_own, P(OWN, None, None), P())
    return jax.shard_map(local, mesh=sub_mesh, in_specs=in_specs, out_specs=out_specs, check_vma=False)
```

```python
import jax
import jax.numpy as jnp
from jax import lax
from jax.sharding import Mesh
from jax.sharding import PartitionSpec as P

stat_decay = 0.9
moment_decay = 0.95
learn_rate = 0.3
adam_eps = 1e-08
norm_eps = 1e-06

GRP = ("yl", "c")
OWN = ("x", "yh", "z")
SUB_SIZES = (4, 2, 4, 2, 8)


def split3(value):
    hi = lax.reduce_precision(value, exponent_bits=8, mantissa_bits=7)
    rest = value - hi
    mid = lax.reduce_precision(rest, exponent_bits=8, mantissa_bits=7)
    lo = lax.reduce_precision(rest - mid, exponent_bits=8, mantissa_bits=7)
    return jnp.stack([hi, mid, lo])


def gather_own_rows(block):
    rows = block.shape[0]
    out = block
    for axis in ("yh", "x", "z"):
        out = lax.all_gather(out, axis, axis=0, tiled=True)
    out = out.reshape(SUB_SIZES[4], SUB_SIZES[2], SUB_SIZES[3], rows, block.shape[1])
    out = jnp.transpose(out, (1, 2, 0, 3, 4))
    return out.reshape(-1, block.shape[1])


def join_cores(parts, cores):
    both = lax.all_to_all(jnp.broadcast_to(parts[None], (cores,) + parts.shape), "c", 0, 0, tiled=True)
    return jnp.transpose(both, (1, 0, 2, 3)).reshape(-1, parts.shape[-1])


def local(activations, out_grads, master, moment, left_root, right_root, stats_in, tile_slot):
    owner_rows = master.shape[0]
    block_size = master.shape[1]
    owners = block_size // owner_rows
    capacity = stats_in.shape[0]
    tile_rows = stats_in.shape[1]
    tile_count = tile_slot.shape[0]
    owner_index = lax.axis_index(OWN)
    grp_size = SUB_SIZES[0] * SUB_SIZES[1]


    partial = lax.dot_general(
        activations, out_grads, (((0,), (0,)), ((), ())), preferred_element_type=jnp.float32
    )
    cores = SUB_SIZES[1]
    part_rows = owner_rows // cores
    halves = jnp.transpose(partial.reshape(owners, cores, part_rows, block_size), (1, 0, 2, 3))
    chip_sum = jnp.sum(lax.all_to_all(halves, "c", 0, 0, tiled=True), axis=0)
    pieces = lax.all_to_all(chip_sum, OWN, 0, 0, tiled=True)
    own_sum = jnp.sum(pieces, axis=0)
    copies = jnp.broadcast_to(own_sum[None], (grp_size, part_rows, block_size))
    got_grp = lax.all_to_all(copies, GRP, 0, 0, tiled=True).reshape(
        SUB_SIZES[0], cores, part_rows, block_size
    )
    grad_rows = jnp.sum(got_grp, axis=0).reshape(owner_rows, block_size)

    moment_out = moment_decay * moment + (1.0 - moment_decay) * grad_rows * grad_rows
    adam_dir = grad_rows / (jnp.sqrt(moment_out) + adam_eps)
    adam_part = split3(jnp.sum(adam_dir * adam_dir))

    extra = jnp.zeros((1, block_size), jnp.float32).at[0, :3].set(adam_part)
    core = lax.axis_index("c")
    my_part = lax.dynamic_slice_in_dim(grad_rows, core * part_rows, part_rows, 0)
    root_part = lax.dynamic_slice_in_dim(right_root, core * part_rows, part_rows, 0)
    payload = jnp.concatenate(
        [my_part.astype(jnp.bfloat16), extra.astype(jnp.bfloat16), root_part], axis=0
    )
    sent = jnp.broadcast_to(payload[None], (owners,) + payload.shape)
    got = lax.all_to_all(sent, OWN, 0, 0, tiled=True)
    adam_sum = jnp.sum(got[:, part_rows, :3].astype(jnp.float32))
    mine = jnp.concatenate([got[:, :part_rows, :], got[:, part_rows + 1 :, :]], axis=1)
    both = lax.all_to_all(jnp.broadcast_to(mine[None], (cores,) + mine.shape), "c", 0, 0, tiled=True)
    both = jnp.transpose(both, (1, 0, 2, 3))
    grad_low = both[:, :, :part_rows, :].reshape(block_size, block_size)
    right_full = both[:, :, part_rows:, :].reshape(block_size, block_size)

    left_mid = jnp.dot(left_root, grad_low, preferred_element_type=jnp.float32).astype(jnp.bfloat16)
    precond = jnp.dot(left_mid, right_full, preferred_element_type=jnp.float32)
    precond_part = jnp.broadcast_to(jnp.sum(precond * precond), (owners, 1, 128))
    precond_sum = jnp.sum(lax.all_to_all(precond_part, OWN, 0, 0, tiled=True)[:, 0, 0])
    graft_scale = jnp.sqrt(adam_sum) / (jnp.sqrt(precond_sum) + norm_eps)
    master_out = master - learn_rate * graft_scale * precond
    weight_part = lax.dynamic_slice_in_dim(master_out.astype(jnp.bfloat16), core * part_rows, part_rows, 0)
    weight_rows = jnp.broadcast_to(weight_part[None], (owners, part_rows, block_size))
    weights = join_cores(lax.all_to_all(weight_rows, OWN, 0, 0, tiled=True), cores)

    my_slots = owner_index * capacity + jnp.arange(capacity, dtype=jnp.int32)
    matches = (tile_slot[:, None] == my_slots[None, :]).astype(jnp.int32)
    tile_ids = jnp.sum(matches * jnp.arange(tile_count, dtype=jnp.int32)[:, None], axis=0)
    filled = jnp.sum(matches, axis=0)
    per_half = block_size // tile_rows
    which_half = tile_ids // per_half
    offsets = (tile_ids - which_half * per_half) * tile_rows
    grad_low_t = grad_low.T
    row_blocks = jnp.concatenate(
        [lax.dynamic_slice_in_dim(grad_low, offsets[s], tile_rows, 0) for s in range(capacity)], axis=0
    )
    col_blocks = jnp.concatenate(
        [lax.dynamic_slice_in_dim(grad_low_t, offsets[s], tile_rows, 0) for s in range(capacity)], axis=0
    )
    left_tiles = lax.dot_general(
        row_blocks, grad_low, (((1,), (1,)), ((), ())), preferred_element_type=jnp.float32
    ).reshape(capacity, tile_rows, block_size)
    right_tiles = jnp.dot(col_blocks, grad_low, preferred_element_type=jnp.float32).reshape(
        capacity, tile_rows, block_size
    )
    product = jnp.where((which_half == 0)[:, None, None], left_tiles, right_tiles)
    fresh = stat_decay * stats_in + (1.0 - stat_decay) / block_size * product
    stats_out = jnp.where((filled > 0)[:, None, None], fresh, 0.0)
    return (master_out, moment_out, stats_out, weights)


def solution(mesh):
    sub_mesh = Mesh(mesh.devices.reshape(SUB_SIZES), GRP + OWN)
    rows_all = P(GRP + OWN, None)
    rows_own = P(OWN, None)
    in_specs = (rows_all, rows_all, rows_own, rows_own, rows_own, rows_own, P(OWN, None, None), P())
    out_specs = (rows_own, rows_own, P(OWN, None, None), P())
    return jax.shard_map(local, mesh=sub_mesh, in_specs=in_specs, out_specs=out_specs, check_vma=False)
```

```python
import jax
import jax.numpy as jnp
from jax import lax
from jax.sharding import Mesh
from jax.sharding import PartitionSpec as P

stat_decay = 0.9
moment_decay = 0.95
learn_rate = 0.3
adam_eps = 1e-08
norm_eps = 1e-06

GRP = ("yl", "c")
OWN = ("x", "yh", "z")
SUB_SIZES = (4, 2, 4, 2, 8)


def gather_own_rows(block):
    rows = block.shape[0]
    out = block
    for axis in ("yh", "x", "z"):
        out = lax.all_gather(out, axis, axis=0, tiled=True)
    out = out.reshape(SUB_SIZES[4], SUB_SIZES[2], SUB_SIZES[3], rows, block.shape[1])
    out = jnp.transpose(out, (1, 2, 0, 3, 4))
    return out.reshape(-1, block.shape[1])


def join_cores(parts, cores):
    both = lax.all_to_all(jnp.broadcast_to(parts[None], (cores,) + parts.shape), "c", 0, 0, tiled=True)
    return jnp.transpose(both, (1, 0, 2, 3)).reshape(-1, parts.shape[-1])


def local(activations, out_grads, master, moment, left_root, right_root, stats_in, tile_slot):
    owner_rows = master.shape[0]
    block_size = master.shape[1]
    owners = block_size // owner_rows
    capacity = stats_in.shape[0]
    tile_rows = stats_in.shape[1]
    tile_count = tile_slot.shape[0]
    owner_index = lax.axis_index(OWN)
    grp_size = SUB_SIZES[0] * SUB_SIZES[1]


    partial = lax.dot_general(
        activations, out_grads, (((0,), (0,)), ((), ())), preferred_element_type=jnp.float32
    )
    cores = SUB_SIZES[1]
    part_rows = owner_rows // cores
    halves = jnp.transpose(partial.reshape(owners, cores, part_rows, block_size), (1, 0, 2, 3))
    chip_sum = jnp.sum(lax.all_to_all(halves, "c", 0, 0, tiled=True), axis=0)
    pieces = lax.all_to_all(chip_sum, OWN, 0, 0, tiled=True)
    own_sum = jnp.sum(pieces, axis=0)
    copies = jnp.broadcast_to(own_sum[None], (grp_size, part_rows, block_size))
    got_grp = lax.all_to_all(copies, GRP, 0, 0, tiled=True).reshape(
        SUB_SIZES[0], cores, part_rows, block_size
    )
    grad_rows = jnp.sum(got_grp, axis=0).reshape(owner_rows, block_size)

    moment_out = moment_decay * moment + (1.0 - moment_decay) * grad_rows * grad_rows
    adam_dir = grad_rows / (jnp.sqrt(moment_out) + adam_eps)
    adam_part = jnp.sum(adam_dir * adam_dir)
    core = lax.axis_index("c")
    my_part = lax.dynamic_slice_in_dim(grad_rows, core * part_rows, part_rows, 0)
    root_part = lax.dynamic_slice_in_dim(right_root, core * part_rows, part_rows, 0)
    payload = jnp.concatenate([my_part.astype(jnp.bfloat16), root_part], axis=0)
    sent = jnp.broadcast_to(payload[None], (owners,) + payload.shape)
    mine = lax.all_to_all(sent, OWN, 0, 0, tiled=True)
    both = lax.all_to_all(jnp.broadcast_to(mine[None], (cores,) + mine.shape), "c", 0, 0, tiled=True)
    both = jnp.transpose(both, (1, 0, 2, 3))
    grad_low = both[:, :, :part_rows, :].reshape(block_size, block_size)
    right_full = both[:, :, part_rows:, :].reshape(block_size, block_size)

    left_mid = jnp.dot(left_root, grad_low, preferred_element_type=jnp.float32).astype(jnp.bfloat16)
    precond = jnp.dot(left_mid, right_full, preferred_element_type=jnp.float32)
    sums = jnp.zeros((1, 128), jnp.float32).at[0, 0].set(jnp.sum(precond * precond)).at[0, 1].set(adam_part)
    got_sums = lax.all_to_all(jnp.broadcast_to(sums[None], (owners, 1, 128)), OWN, 0, 0, tiled=True)
    precond_sum = jnp.sum(got_sums[:, 0, 0])
    adam_sum = jnp.sum(got_sums[:, 0, 1])
    graft_scale = jnp.sqrt(adam_sum) / (jnp.sqrt(precond_sum) + norm_eps)
    master_out = master - learn_rate * graft_scale * precond
    weight_part = lax.dynamic_slice_in_dim(master_out.astype(jnp.bfloat16), core * part_rows, part_rows, 0)
    weight_rows = jnp.broadcast_to(weight_part[None], (owners, part_rows, block_size))
    weights = join_cores(lax.all_to_all(weight_rows, OWN, 0, 0, tiled=True), cores)

    my_slots = owner_index * capacity + jnp.arange(capacity, dtype=jnp.int32)
    matches = (tile_slot[:, None] == my_slots[None, :]).astype(jnp.int32)
    tile_ids = jnp.sum(matches * jnp.arange(tile_count, dtype=jnp.int32)[:, None], axis=0)
    filled = jnp.sum(matches, axis=0)
    per_half = block_size // tile_rows
    which_half = tile_ids // per_half
    offsets = (tile_ids - which_half * per_half) * tile_rows
    grad_low_t = grad_low.T
    row_blocks = jnp.concatenate(
        [lax.dynamic_slice_in_dim(grad_low, offsets[s], tile_rows, 0) for s in range(capacity)], axis=0
    )
    col_blocks = jnp.concatenate(
        [lax.dynamic_slice_in_dim(grad_low_t, offsets[s], tile_rows, 0) for s in range(capacity)], axis=0
    )
    left_tiles = lax.dot_general(
        row_blocks, grad_low, (((1,), (1,)), ((), ())), preferred_element_type=jnp.float32
    ).reshape(capacity, tile_rows, block_size)
    right_tiles = jnp.dot(col_blocks, grad_low, preferred_element_type=jnp.float32).reshape(
        capacity, tile_rows, block_size
    )
    product = jnp.where((which_half == 0)[:, None, None], left_tiles, right_tiles)
    fresh = stat_decay * stats_in + (1.0 - stat_decay) / block_size * product
    stats_out = jnp.where((filled > 0)[:, None, None], fresh, 0.0)
    return (master_out, moment_out, stats_out, weights)


def solution(mesh):
    sub_mesh = Mesh(mesh.devices.reshape(SUB_SIZES), GRP + OWN)
    rows_all = P(GRP + OWN, None)
    rows_own = P(OWN, None)
    in_specs = (rows_all, rows_all, rows_own, rows_own, rows_own, rows_own, P(OWN, None, None), P())
    out_specs = (rows_own, rows_own, P(OWN, None, None), P())
    return jax.shard_map(local, mesh=sub_mesh, in_specs=in_specs, out_specs=out_specs, check_vma=False)
```

```python
import jax
import jax.numpy as jnp
from jax import lax
from jax.sharding import Mesh
from jax.sharding import PartitionSpec as P

stat_decay = 0.9
moment_decay = 0.95
learn_rate = 0.3
adam_eps = 1e-08
norm_eps = 1e-06

GRP = ("yl", "c")
OWN = ("x", "yh", "z")
SUB_SIZES = (4, 2, 4, 2, 8)


def gather_own_rows(block):
    rows = block.shape[0]
    out = block
    for axis in ("yh", "x", "z"):
        out = lax.all_gather(out, axis, axis=0, tiled=True)
    out = out.reshape(SUB_SIZES[4], SUB_SIZES[2], SUB_SIZES[3], rows, block.shape[1])
    out = jnp.transpose(out, (1, 2, 0, 3, 4))
    return out.reshape(-1, block.shape[1])


def join_cores(parts, cores):
    both = lax.all_to_all(jnp.broadcast_to(parts[None], (cores,) + parts.shape), "c", 0, 0, tiled=True)
    return jnp.transpose(both, (1, 0, 2, 3)).reshape(-1, parts.shape[-1])


def local(activations, out_grads, master, moment, left_root, right_root, stats_in, tile_slot):
    owner_rows = master.shape[0]
    block_size = master.shape[1]
    owners = block_size // owner_rows
    capacity = stats_in.shape[0]
    tile_rows = stats_in.shape[1]
    tile_count = tile_slot.shape[0]
    owner_index = lax.axis_index(OWN)
    grp_size = SUB_SIZES[0] * SUB_SIZES[1]


    partial = lax.dot_general(
        activations, out_grads, (((0,), (0,)), ((), ())), preferred_element_type=jnp.float32
    )
    cores = SUB_SIZES[1]
    lows = SUB_SIZES[0]
    part_rows = owner_rows // cores
    bit_rows = part_rows // lows
    split = partial.reshape(owners, cores, lows, bit_rows, block_size)
    halves = jnp.transpose(split, (1, 0, 2, 3, 4))
    chip_sum = jnp.sum(lax.all_to_all(halves, "c", 0, 0, tiled=True), axis=0)
    quarters = jnp.transpose(chip_sum, (1, 0, 2, 3))
    low_sum = jnp.sum(lax.all_to_all(quarters, "yl", 0, 0, tiled=True), axis=0)
    own_sum = jnp.sum(lax.all_to_all(low_sum, OWN, 0, 0, tiled=True), axis=0)
    copies = jnp.broadcast_to(own_sum[None], (grp_size, bit_rows, block_size))
    got_grp = lax.all_to_all(copies, GRP, 0, 0, tiled=True).reshape(lows, cores, bit_rows, block_size)
    grad_rows = jnp.transpose(got_grp, (1, 0, 2, 3)).reshape(owner_rows, block_size)

    moment_out = moment_decay * moment + (1.0 - moment_decay) * grad_rows * grad_rows
    adam_dir = grad_rows / (jnp.sqrt(moment_out) + adam_eps)
    adam_part = jnp.sum(adam_dir * adam_dir)
    core = lax.axis_index("c")
    my_part = lax.dynamic_slice_in_dim(grad_rows, core * part_rows, part_rows, 0)
    root_part = lax.dynamic_slice_in_dim(right_root, core * part_rows, part_rows, 0)
    payload = jnp.concatenate([my_part.astype(jnp.bfloat16), root_part], axis=0)
    sent = jnp.broadcast_to(payload[None], (owners,) + payload.shape)
    mine = lax.all_to_all(sent, OWN, 0, 0, tiled=True)
    both = lax.all_to_all(jnp.broadcast_to(mine[None], (cores,) + mine.shape), "c", 0, 0, tiled=True)
    both = jnp.transpose(both, (1, 0, 2, 3))
    grad_low = both[:, :, :part_rows, :].reshape(block_size, block_size)
    right_full = both[:, :, part_rows:, :].reshape(block_size, block_size)

    left_mid = jnp.dot(left_root, grad_low, preferred_element_type=jnp.float32).astype(jnp.bfloat16)
    precond = jnp.dot(left_mid, right_full, preferred_element_type=jnp.float32)
    sums = jnp.zeros((1, 128), jnp.float32).at[0, 0].set(jnp.sum(precond * precond)).at[0, 1].set(adam_part)
    got_sums = lax.all_to_all(jnp.broadcast_to(sums[None], (owners, 1, 128)), OWN, 0, 0, tiled=True)
    precond_sum = jnp.sum(got_sums[:, 0, 0])
    adam_sum = jnp.sum(got_sums[:, 0, 1])
    graft_scale = jnp.sqrt(adam_sum) / (jnp.sqrt(precond_sum) + norm_eps)
    master_out = master - learn_rate * graft_scale * precond
    weight_part = lax.dynamic_slice_in_dim(master_out.astype(jnp.bfloat16), core * part_rows, part_rows, 0)
    weight_rows = jnp.broadcast_to(weight_part[None], (owners, part_rows, block_size))
    weights = join_cores(lax.all_to_all(weight_rows, OWN, 0, 0, tiled=True), cores)

    my_slots = owner_index * capacity + jnp.arange(capacity, dtype=jnp.int32)
    matches = (tile_slot[:, None] == my_slots[None, :]).astype(jnp.int32)
    tile_ids = jnp.sum(matches * jnp.arange(tile_count, dtype=jnp.int32)[:, None], axis=0)
    filled = jnp.sum(matches, axis=0)
    per_half = block_size // tile_rows
    which_half = tile_ids // per_half
    offsets = (tile_ids - which_half * per_half) * tile_rows
    grad_low_t = grad_low.T
    row_blocks = jnp.concatenate(
        [lax.dynamic_slice_in_dim(grad_low, offsets[s], tile_rows, 0) for s in range(capacity)], axis=0
    )
    col_blocks = jnp.concatenate(
        [lax.dynamic_slice_in_dim(grad_low_t, offsets[s], tile_rows, 0) for s in range(capacity)], axis=0
    )
    left_tiles = lax.dot_general(
        row_blocks, grad_low, (((1,), (1,)), ((), ())), preferred_element_type=jnp.float32
    ).reshape(capacity, tile_rows, block_size)
    right_tiles = jnp.dot(col_blocks, grad_low, preferred_element_type=jnp.float32).reshape(
        capacity, tile_rows, block_size
    )
    product = jnp.where((which_half == 0)[:, None, None], left_tiles, right_tiles)
    fresh = stat_decay * stats_in + (1.0 - stat_decay) / block_size * product
    stats_out = jnp.where((filled > 0)[:, None, None], fresh, 0.0)
    return (master_out, moment_out, stats_out, weights)


def solution(mesh):
    sub_mesh = Mesh(mesh.devices.reshape(SUB_SIZES), GRP + OWN)
    rows_all = P(GRP + OWN, None)
    rows_own = P(OWN, None)
    in_specs = (rows_all, rows_all, rows_own, rows_own, rows_own, rows_own, P(OWN, None, None), P())
    out_specs = (rows_own, rows_own, P(OWN, None, None), P())
    return jax.shard_map(local, mesh=sub_mesh, in_specs=in_specs, out_specs=out_specs, check_vma=False)
```

```python
import jax
import jax.numpy as jnp
from jax import lax
from jax.sharding import Mesh
from jax.sharding import PartitionSpec as P

stat_decay = 0.9
moment_decay = 0.95
learn_rate = 0.3
adam_eps = 1e-08
norm_eps = 1e-06

GRP = ("yl", "c")
OWN = ("x", "yh", "z")
SUB_SIZES = (4, 2, 4, 2, 8)


def gather_own_rows(block):
    rows = block.shape[0]
    out = block
    for axis in ("yh", "x", "z"):
        out = lax.all_gather(out, axis, axis=0, tiled=True)
    out = out.reshape(SUB_SIZES[4], SUB_SIZES[2], SUB_SIZES[3], rows, block.shape[1])
    out = jnp.transpose(out, (1, 2, 0, 3, 4))
    return out.reshape(-1, block.shape[1])


def join_cores(parts, cores):
    both = lax.all_to_all(jnp.broadcast_to(parts[None], (cores,) + parts.shape), "c", 0, 0, tiled=True)
    return jnp.transpose(both, (1, 0, 2, 3)).reshape(-1, parts.shape[-1])


def local(activations, out_grads, master, moment, left_root, right_root, stats_in, tile_slot):
    owner_rows = master.shape[0]
    block_size = master.shape[1]
    owners = block_size // owner_rows
    capacity = stats_in.shape[0]
    tile_rows = stats_in.shape[1]
    tile_count = tile_slot.shape[0]
    owner_index = lax.axis_index(OWN)
    grp_size = SUB_SIZES[0] * SUB_SIZES[1]


    cores_r = SUB_SIZES[1]
    root_part = lax.dynamic_slice_in_dim(
        right_root, lax.axis_index("c") * (owner_rows // cores_r), owner_rows // cores_r, 0
    )
    roots_got = lax.all_to_all(
        jnp.broadcast_to(root_part[None], (owners,) + root_part.shape), OWN, 0, 0, tiled=True
    )
    partial = lax.dot_general(
        activations, out_grads, (((0,), (0,)), ((), ())), preferred_element_type=jnp.float32
    )
    cores = SUB_SIZES[1]
    part_rows = owner_rows // cores
    halves = jnp.transpose(partial.reshape(owners, cores, part_rows, block_size), (1, 0, 2, 3))
    chip_sum = jnp.sum(lax.all_to_all(halves, "c", 0, 0, tiled=True), axis=0)
    pieces = lax.all_to_all(chip_sum, OWN, 0, 0, tiled=True)
    own_sum = jnp.sum(pieces, axis=0)
    copies = jnp.broadcast_to(own_sum[None], (grp_size, part_rows, block_size))
    got_grp = lax.all_to_all(copies, GRP, 0, 0, tiled=True).reshape(
        SUB_SIZES[0], cores, part_rows, block_size
    )
    grad_rows = jnp.sum(got_grp, axis=0).reshape(owner_rows, block_size)

    moment_out = moment_decay * moment + (1.0 - moment_decay) * grad_rows * grad_rows
    adam_dir = grad_rows / (jnp.sqrt(moment_out) + adam_eps)
    adam_part = jnp.sum(adam_dir * adam_dir)
    core = lax.axis_index("c")
    my_part = lax.dynamic_slice_in_dim(grad_rows, core * part_rows, part_rows, 0)
    payload = my_part.astype(jnp.bfloat16)
    sent = jnp.broadcast_to(payload[None], (owners,) + payload.shape)
    mine = jnp.concatenate([lax.all_to_all(sent, OWN, 0, 0, tiled=True), roots_got], axis=1)
    both = lax.all_to_all(jnp.broadcast_to(mine[None], (cores,) + mine.shape), "c", 0, 0, tiled=True)
    both = jnp.transpose(both, (1, 0, 2, 3))
    grad_low = both[:, :, :part_rows, :].reshape(block_size, block_size)
    right_full = both[:, :, part_rows:, :].reshape(block_size, block_size)

    left_mid = jnp.dot(left_root, grad_low, preferred_element_type=jnp.float32).astype(jnp.bfloat16)
    precond = jnp.dot(left_mid, right_full, preferred_element_type=jnp.float32)
    sums = jnp.zeros((1, 128), jnp.float32).at[0, 0].set(jnp.sum(precond * precond)).at[0, 1].set(adam_part)
    got_sums = lax.all_to_all(jnp.broadcast_to(sums[None], (owners, 1, 128)), OWN, 0, 0, tiled=True)
    precond_sum = jnp.sum(got_sums[:, 0, 0])
    adam_sum = jnp.sum(got_sums[:, 0, 1])
    graft_scale = jnp.sqrt(adam_sum) / (jnp.sqrt(precond_sum) + norm_eps)
    master_out = master - learn_rate * graft_scale * precond
    weight_part = lax.dynamic_slice_in_dim(master_out.astype(jnp.bfloat16), core * part_rows, part_rows, 0)
    weight_rows = jnp.broadcast_to(weight_part[None], (owners, part_rows, block_size))
    weights = join_cores(lax.all_to_all(weight_rows, OWN, 0, 0, tiled=True), cores)

    my_slots = owner_index * capacity + jnp.arange(capacity, dtype=jnp.int32)
    matches = (tile_slot[:, None] == my_slots[None, :]).astype(jnp.int32)
    tile_ids = jnp.sum(matches * jnp.arange(tile_count, dtype=jnp.int32)[:, None], axis=0)
    filled = jnp.sum(matches, axis=0)
    per_half = block_size // tile_rows
    which_half = tile_ids // per_half
    offsets = (tile_ids - which_half * per_half) * tile_rows
    grad_low_t = grad_low.T
    row_blocks = jnp.concatenate(
        [lax.dynamic_slice_in_dim(grad_low, offsets[s], tile_rows, 0) for s in range(capacity)], axis=0
    )
    col_blocks = jnp.concatenate(
        [lax.dynamic_slice_in_dim(grad_low_t, offsets[s], tile_rows, 0) for s in range(capacity)], axis=0
    )
    left_tiles = lax.dot_general(
        row_blocks, grad_low, (((1,), (1,)), ((), ())), preferred_element_type=jnp.float32
    ).reshape(capacity, tile_rows, block_size)
    right_tiles = jnp.dot(col_blocks, grad_low, preferred_element_type=jnp.float32).reshape(
        capacity, tile_rows, block_size
    )
    product = jnp.where((which_half == 0)[:, None, None], left_tiles, right_tiles)
    fresh = stat_decay * stats_in + (1.0 - stat_decay) / block_size * product
    stats_out = jnp.where((filled > 0)[:, None, None], fresh, 0.0)
    return (master_out, moment_out, stats_out, weights)


def solution(mesh):
    sub_mesh = Mesh(mesh.devices.reshape(SUB_SIZES), GRP + OWN)
    rows_all = P(GRP + OWN, None)
    rows_own = P(OWN, None)
    in_specs = (rows_all, rows_all, rows_own, rows_own, rows_own, rows_own, P(OWN, None, None), P())
    out_specs = (rows_own, rows_own, P(OWN, None, None), P())
    return jax.shard_map(local, mesh=sub_mesh, in_specs=in_specs, out_specs=out_specs, check_vma=False)
```
